512 devices in a mesh: ch: 128 (over z, x, y_lo), af: 4 (over y_hi, core).
Axes of the slice: x: 4, y: 4 (y_hi: 2, y_lo: 2; y = y_hi * 2 + y_lo), z: 16, core: 2. Of those that a mesh axis runs over, the one named last changes fastest.
Arguments:
- records: bfloat16 [128, 8192, 1024], P('ch', 'af'), may hold values from -80 to 80
- quality: int32 [1024], replicated, may hold values 0 or 1
- band_low: int32 [1024], P('ch'), may hold values from 0 to 31
- band_high: int32 [1024], P('ch'), may hold values from 96 to 128
Outputs:
- cross_spectra: float32 [1024, 129, 2, 512], P('ch', None, None, 'af')
The draws below stay inside these ranges and needn't reach their ends.
All inputs are finite; a program needn't handle non-finite values.
Results may differ from the reference program's by a relative error of at most 0.0054.
Values may be sent and summed in bfloat16 or wider, within the bound.
No kernel may reach another device: no remote copies, remote signals or barrier semaphores. Data moves between devices by JAX's collectives and lax.ppermute only.
A program may use at most 64 MiB of HBM per device.

```python
import math
import jax
import jax.numpy as jnp
from jax import lax

SEGLEN = 8192
BINS = 512
LOWBIN = 64
SMOOTH = 32
REACH = 128
CHANNELS = 1024
SEGS = 128


def draw_records(key, part):
    base_key = jax.random.fold_in(key, 11)
    noise_key, chan_key, seg_key = jax.random.split(base_key, 3)
    noise_draw = jnp.clip(jax.random.normal(noise_key, (SEGS, SEGLEN, CHANNELS), jnp.float32), -4.0, 4.0)
    chan_scale = jnp.exp(jax.random.uniform(chan_key, (1, 1, CHANNELS), jnp.float32) * math.log(10.0))
    seg_scale = jnp.exp(jax.random.uniform(seg_key, (SEGS, 1, 1), jnp.float32) * math.log(2.0))
    return (noise_draw * chan_scale * seg_scale).astype(jnp.bfloat16)


def with_ends(result, rng, smallest, high):
    spot = [jax.random.randint(jax.random.fold_in(rng, axis), (), 0, length) for axis, length in enumerate(result.shape)]
    main_axis = result.shape.index(max(result.shape))
    beside = spot[:main_axis] + [(spot[main_axis] + 1) % result.shape[main_axis]] + spot[main_axis + 1:]
    return result.at[tuple(spot)].set(smallest).at[tuple(beside)].set(high)


def setup_inputs(seed: int = 0) -> dict:
    splits = jax.random.split(jax.random.key(seed), 5)
    return {
        "records": draw_records(jax.random.fold_in(splits[4], 71), 0),
        "quality": with_ends((jax.random.randint(splits[1], (CHANNELS,), 0, 8) < 7).astype(jnp.int32), jax.random.fold_in(splits[1], 1), 0, 1),
        "band_low": with_ends(jax.random.randint(splits[2], (CHANNELS,), 0, REACH // 4), jax.random.fold_in(splits[2], 1), 0, (REACH // 4) - 1).astype(jnp.int32),
        "band_high": with_ends(jax.random.randint(splits[3], (CHANNELS,), REACH - REACH // 4, REACH + 1), jax.random.fold_in(splits[3], 1), REACH - REACH // 4, REACH).astype(jnp.int32),
    }


def taper_table(bin_index, sample_index, length):
    phase_index = bin_index[:, None] * sample_index[None, :] % length
    angles = phase_index.astype(jnp.float32) * (2.0 * math.pi / length)
    tapers = 0.5 - 0.5 * jnp.cos(sample_index.astype(jnp.float32) * (2.0 * math.pi / length))
    real_row = (tapers[None, :] * jnp.cos(angles)).astype(jnp.bfloat16)
    imag_row = (-(tapers[None, :] * jnp.sin(angles))).astype(jnp.bfloat16)
    return jnp.stack([real_row, imag_row], axis=1)

def band_sum(padded, half_width):
    row_count = padded.shape[0] - 2 * half_width
    row_ids = jnp.arange(row_count, dtype=jnp.int32)[:, None]
    col_ids = jnp.arange(padded.shape[0], dtype=jnp.int32)[None, :]
    band_matrix = ((col_ids >= row_ids) & (col_ids <= row_ids + 2 * half_width)).astype(jnp.float32)
    return jnp.dot(band_matrix, padded, precision=lax.Precision.HIGHEST, preferred_element_type=jnp.float32)

def reference(records, quality, band_low, band_high):
    bin_index = LOWBIN + jnp.arange(BINS, dtype=jnp.int32)
    sample_index = jnp.arange(SEGLEN, dtype=jnp.int32)
    basis_table = taper_table(bin_index, sample_index, SEGLEN).reshape(2 * BINS, SEGLEN)
    scaling = quality.astype(jnp.float32)

    def whiten(segment):
        spectra = jnp.dot(basis_table, segment, preferred_element_type=jnp.float32).reshape(BINS, 2, CHANNELS)
        power_bins = spectra[:, 0] * spectra[:, 0] + spectra[:, 1] * spectra[:, 1]
        padded = jnp.pad(power_bins, ((SMOOTH, SMOOTH), (0, 0)))
        smoothed = band_sum(padded, SMOOTH)
        factor = scaling[None, :] / jnp.sqrt(smoothed * (1.0 / (2 * SMOOTH + 1)) + 1e-06)
        return (spectra * factor[:, None, :]).astype(jnp.bfloat16)
    whitened = lax.map(whiten, records)
    whitened_wide = whitened.astype(jnp.float32)
    padded_wide = jnp.pad(whitened_wide, ((0, 0), (0, 0), (0, 0), (0, REACH)))

    def one_offset(offset):
        shifted = lax.dynamic_slice_in_dim(padded_wide, offset, CHANNELS, 3)
        real_part = lax.optimization_barrier(jnp.sum(whitened_wide[:, :, 0] * shifted[:, :, 0] + whitened_wide[:, :, 1] * shifted[:, :, 1], axis=0))
        imag_part = lax.optimization_barrier(jnp.sum(whitened_wide[:, :, 1] * shifted[:, :, 0] - whitened_wide[:, :, 0] * shifted[:, :, 1], axis=0))
        return jnp.stack([real_part, imag_part], axis=0)
    offsets = jnp.arange(REACH + 1, dtype=jnp.int32)
    stacked = lax.map(one_offset, offsets)
    cross_all = jnp.transpose(stacked, (3, 0, 1, 2))
    inside_band = ((offsets[None, :] >= band_low[:, None]) & (offsets[None, :] <= band_high[:, None])).astype(jnp.float32)
    return cross_all * inside_band[:, :, None, None] * (1.0 / math.sqrt(SEGS))
```

```python
import math

import jax
import jax.numpy as jnp
from jax import lax
from jax.sharding import PartitionSpec as P

SEGLEN = 8192
BINS = 512
LOWBIN = 64
SMOOTH = 32
REACH = 128


def extended(cells, sides, width):
    for axis, dim in sides:
        count = lax.axis_size(axis)
        ends = count - 1
        head = lax.slice_in_dim(cells, 0, width, axis=dim)
        tail = lax.slice_in_dim(cells, cells.shape[dim] - width, cells.shape[dim], axis=dim)
        cells = jnp.concatenate(
            [
                lax.ppermute(tail, axis, [(i, (i + 1) % count) for i in range(ends)]),
                cells,
                lax.ppermute(head, axis, [((i + 1) % count, i) for i in range(ends)]),
            ],
            axis=dim,
        )
    return cells


def taper_table(bin_index, sample_index, length):
    phase_index = bin_index[:, None] * sample_index[None, :] % length
    angles = phase_index.astype(jnp.float32) * (2.0 * math.pi / length)
    tapers = 0.5 - 0.5 * jnp.cos(sample_index.astype(jnp.float32) * (2.0 * math.pi / length))
    real_row = (tapers[None, :] * jnp.cos(angles)).astype(jnp.bfloat16)
    imag_row = (-(tapers[None, :] * jnp.sin(angles))).astype(jnp.bfloat16)
    return jnp.stack([real_row, imag_row], axis=1)


def band_sum(padded, half_width):
    row_count = padded.shape[0] - 2 * half_width
    row_ids = jnp.arange(row_count, dtype=jnp.int32)[:, None]
    col_ids = jnp.arange(padded.shape[0], dtype=jnp.int32)[None, :]
    band_matrix = ((col_ids >= row_ids) & (col_ids <= row_ids + 2 * half_width)).astype(jnp.float32)
    return jnp.dot(
        band_matrix, padded, precision=lax.Precision.HIGHEST, preferred_element_type=jnp.float32
    )


def whiten_local(records, quality):
    local_record = records[0]
    quarter = local_record.shape[0]
    channels = local_record.shape[1]
    parts = lax.axis_size("af")
    band_rows = BINS // parts
    sample_index = lax.axis_index("af") * quarter + jnp.arange(quarter, dtype=jnp.int32)
    bin_index = LOWBIN + jnp.arange(BINS, dtype=jnp.int32)
    basis_table = taper_table(bin_index, sample_index, SEGLEN).reshape(2 * BINS, quarter)
    spectra = lax.psum_scatter(
        jnp.dot(basis_table, local_record, preferred_element_type=jnp.float32).reshape(
            BINS, 2, channels
        ),
        "af",
        scatter_dimension=0,
        tiled=True,
    )
    power_bins = spectra[:, 0] * spectra[:, 0] + spectra[:, 1] * spectra[:, 1]
    padded = extended(power_bins, (("af", 0),), SMOOTH)
    smoothed = band_sum(padded, SMOOTH)
    factor = quality.astype(jnp.float32)[None, :] / jnp.sqrt(
        smoothed * (1.0 / (2 * SMOOTH + 1)) + 1e-06
    )
    return (spectra * factor[:, None, :]).astype(jnp.bfloat16)


def bin_cross(whitened, block):
    segs, _, channels = whitened.shape
    blocks = channels // block
    real_w = whitened[:, 0]
    imag_w = whitened[:, 1]
    right = jnp.concatenate([real_w, imag_w], axis=0)
    left = jnp.stack([right, jnp.concatenate([imag_w, -real_w], axis=0)], axis=0)
    depth = right.shape[0]
    right_pad = jnp.pad(right, ((0, 0), (0, block))).reshape(depth, blocks + 1, block)
    windows = jnp.concatenate([right_pad[:, :blocks], right_pad[:, 1:]], axis=2)
    left_blocks = left.reshape(2, depth, blocks, block)
    gram = jnp.einsum(
        "pkbc,kbe->bcpe", left_blocks, windows, preferred_element_type=jnp.float32
    )
    width = 2 * block
    flat = gram.transpose(0, 2, 1, 3).reshape(blocks, 2, block * width)
    flat = jnp.pad(flat, ((0, 0), (0, 0), (0, block)))
    skew = flat.reshape(blocks, 2, block, width + 1)[:, :, :, : REACH + 1]
    return skew.transpose(0, 2, 3, 1).reshape(channels, REACH + 1, 2)


def per_device(records, quality, band_low, band_high):
    whitened = whiten_local(records, quality)
    band_rows, _, channels = whitened.shape
    slab_count = lax.axis_size("ch")
    slab_width = channels // slab_count
    by_bin = lax.all_to_all(
        whitened.reshape(band_rows, 1, 2, channels),
        "ch",
        split_axis=0,
        concat_axis=1,
        tiled=True,
    )[0]
    segments = by_bin.shape[0]
    cross = bin_cross(by_bin, REACH)
    back = lax.all_to_all(
        cross.reshape(slab_count, slab_width, REACH + 1, 2),
        "ch",
        split_axis=0,
        concat_axis=0,
        tiled=True,
    )
    offsets = jnp.arange(REACH + 1, dtype=jnp.int32)
    inside_band = (
        (offsets[None, :] >= band_low[:, None]) & (offsets[None, :] <= band_high[:, None])
    ).astype(jnp.float32)
    result = (
        jnp.transpose(back, (1, 2, 3, 0))
        * inside_band[:, :, None, None]
        * (1.0 / math.sqrt(segments))
    )
    return result


def solution(mesh):
    return jax.shard_map(
        per_device,
        mesh=mesh,
        in_specs=(P("ch", "af", None), P(), P("ch"), P("ch")),
        out_specs=P("ch", None, None, "af"),
        check_vma=False,
    )
```

```python
import math

import jax
import jax.numpy as jnp
from jax import lax
from jax.sharding import PartitionSpec as P

SEGLEN = 8192
BINS = 512
LOWBIN = 64
SMOOTH = 32
REACH = 128


def extended(cells, sides, width):
    for axis, dim in sides:
        count = lax.axis_size(axis)
        ends = count - 1
        head = lax.slice_in_dim(cells, 0, width, axis=dim)
        tail = lax.slice_in_dim(cells, cells.shape[dim] - width, cells.shape[dim], axis=dim)
        cells = jnp.concatenate(
            [
                lax.ppermute(tail, axis, [(i, (i + 1) % count) for i in range(ends)]),
                cells,
                lax.ppermute(head, axis, [((i + 1) % count, i) for i in range(ends)]),
            ],
            axis=dim,
        )
    return cells


def taper_table(bin_index, sample_start, quarter, length):
    fine = 64
    coarse = quarter // fine
    step = 2.0 * math.pi / length
    coarse_t = sample_start + fine * jnp.arange(coarse, dtype=jnp.int32)
    fine_t = jnp.arange(fine, dtype=jnp.int32)
    coarse_angle = (bin_index[:, None] * coarse_t[None, :] % length).astype(jnp.float32) * step
    fine_angle = (bin_index[:, None] * fine_t[None, :] % length).astype(jnp.float32) * step
    cos_c = jnp.cos(coarse_angle)[:, :, None]
    sin_c = jnp.sin(coarse_angle)[:, :, None]
    cos_f = jnp.cos(fine_angle)[:, None, :]
    sin_f = jnp.sin(fine_angle)[:, None, :]
    rows = bin_index.shape[0]
    cos_a = (cos_c * cos_f - sin_c * sin_f).reshape(rows, quarter)
    sin_a = (sin_c * cos_f + cos_c * sin_f).reshape(rows, quarter)
    sample_index = sample_start + jnp.arange(quarter, dtype=jnp.int32)
    tapers = 0.5 - 0.5 * jnp.cos(sample_index.astype(jnp.float32) * step)
    real_row = (tapers[None, :] * cos_a).astype(jnp.bfloat16)
    imag_row = (-(tapers[None, :] * sin_a)).astype(jnp.bfloat16)
    return jnp.stack([real_row, imag_row], axis=1)


def band_sum(padded, half_width):
    row_count = padded.shape[0] - 2 * half_width
    row_ids = jnp.arange(row_count, dtype=jnp.int32)[:, None]
    col_ids = jnp.arange(padded.shape[0], dtype=jnp.int32)[None, :]
    band_matrix = ((col_ids >= row_ids) & (col_ids <= row_ids + 2 * half_width)).astype(jnp.float32)
    return jnp.dot(
        band_matrix, padded, precision=lax.Precision.HIGHEST, preferred_element_type=jnp.float32
    )


def whiten_local(records, quality):
    local_record = records[0]
    quarter = local_record.shape[0]
    channels = local_record.shape[1]
    parts = lax.axis_size("af")
    band_rows = BINS // parts
    sample_start = lax.axis_index("af") * quarter
    bin_index = LOWBIN + jnp.arange(BINS, dtype=jnp.int32)
    basis_table = taper_table(bin_index, sample_start, quarter, SEGLEN).reshape(2 * BINS, quarter)
    spectra = lax.psum_scatter(
        jnp.dot(basis_table, local_record, preferred_element_type=jnp.float32).reshape(
            BINS, 2, channels
        ),
        "af",
        scatter_dimension=0,
        tiled=True,
    )
    power_bins = spectra[:, 0] * spectra[:, 0] + spectra[:, 1] * spectra[:, 1]
    padded = extended(power_bins, (("af", 0),), SMOOTH)
    smoothed = band_sum(padded, SMOOTH)
    factor = quality.astype(jnp.float32)[None, :] / jnp.sqrt(
        smoothed * (1.0 / (2 * SMOOTH + 1)) + 1e-06
    )
    return (spectra * factor[:, None, :]).astype(jnp.bfloat16)


def bin_cross(whitened, block):
    segs, _, channels = whitened.shape
    blocks = channels // block
    real_w = whitened[:, 0]
    imag_w = whitened[:, 1]
    right = jnp.concatenate([real_w, imag_w], axis=0)
    left = jnp.stack([right, jnp.concatenate([imag_w, -real_w], axis=0)], axis=0)
    depth = right.shape[0]
    right_pad = jnp.pad(right, ((0, 0), (0, block))).reshape(depth, blocks + 1, block)
    windows = jnp.concatenate([right_pad[:, :blocks], right_pad[:, 1:]], axis=2)
    left_blocks = left.reshape(2, depth, blocks, block)
    gram = jnp.einsum(
        "pkbc,kbe->bcpe", left_blocks, windows, preferred_element_type=jnp.float32
    )
    width = 2 * block
    flat = gram.transpose(0, 2, 1, 3).reshape(blocks, 2, block * width)
    flat = jnp.pad(flat, ((0, 0), (0, 0), (0, block)))
    skew = flat.reshape(blocks, 2, block, width + 1)[:, :, :, : REACH + 1]
    return skew.transpose(0, 2, 3, 1).reshape(channels, REACH + 1, 2)


def per_device(records, quality, band_low, band_high):
    whitened = whiten_local(records, quality)
    band_rows, _, channels = whitened.shape
    slab_count = lax.axis_size("ch")
    slab_width = channels // slab_count
    by_bin = lax.all_to_all(
        whitened.reshape(band_rows, 1, 2, channels),
        "ch",
        split_axis=0,
        concat_axis=1,
        tiled=True,
    )[0]
    segments = by_bin.shape[0]
    cross = bin_cross(by_bin, REACH)
    back = lax.all_to_all(
        cross.astype(jnp.bfloat16).reshape(slab_count, slab_width, REACH + 1, 2),
        "ch",
        split_axis=0,
        concat_axis=0,
        tiled=True,
    ).astype(jnp.float32)
    offsets = jnp.arange(REACH + 1, dtype=jnp.int32)
    inside_band = (
        (offsets[None, :] >= band_low[:, None]) & (offsets[None, :] <= band_high[:, None])
    ).astype(jnp.float32)
    result = (
        jnp.transpose(back, (1, 2, 3, 0))
        * inside_band[:, :, None, None]
        * (1.0 / math.sqrt(segments))
    )
    return result


def solution(mesh):
    return jax.shard_map(
        per_device,
        mesh=mesh,
        in_specs=(P("ch", "af", None), P(), P("ch"), P("ch")),
        out_specs=P("ch", None, None, "af"),
        check_vma=False,
    )
```

```python
import math

import jax
import jax.numpy as jnp
from jax import lax
from jax.sharding import PartitionSpec as P

SEGLEN = 8192
BINS = 512
LOWBIN = 64
SMOOTH = 32
REACH = 128


def extended(cells, sides, width):
    for axis, dim in sides:
        count = lax.axis_size(axis)
        ends = count - 1
        head = lax.slice_in_dim(cells, 0, width, axis=dim)
        tail = lax.slice_in_dim(cells, cells.shape[dim] - width, cells.shape[dim], axis=dim)
        cells = jnp.concatenate(
            [
                lax.ppermute(tail, axis, [(i, (i + 1) % count) for i in range(ends)]),
                cells,
                lax.ppermute(head, axis, [((i + 1) % count, i) for i in range(ends)]),
            ],
            axis=dim,
        )
    return cells


def taper_table(bin_start, sample_index, length):
    fine = 64
    groups = 8
    step = 2.0 * math.pi / length
    coarse_bins = bin_start + fine * jnp.arange(groups, dtype=jnp.int32)
    fine_bins = jnp.arange(fine, dtype=jnp.int32)
    coarse_angle = (coarse_bins[:, None] * sample_index[None, :] % length).astype(jnp.float32) * step
    fine_angle = (fine_bins[:, None] * sample_index[None, :] % length).astype(jnp.float32) * step
    cos_c = jnp.cos(coarse_angle)[:, None, :]
    sin_c = jnp.sin(coarse_angle)[:, None, :]
    cos_f = jnp.cos(fine_angle)[None, :, :]
    sin_f = jnp.sin(fine_angle)[None, :, :]
    rows = groups * fine
    cos_a = (cos_c * cos_f - sin_c * sin_f).reshape(rows, -1)
    sin_a = (sin_c * cos_f + cos_c * sin_f).reshape(rows, -1)
    tapers = 0.5 - 0.5 * jnp.cos(sample_index.astype(jnp.float32) * step)
    real_row = (tapers[None, :] * cos_a).astype(jnp.bfloat16)
    imag_row = (-(tapers[None, :] * sin_a)).astype(jnp.bfloat16)
    return jnp.stack([real_row, imag_row], axis=1)


def reduce_scatter_af(partial):
    index = lax.axis_index("af")
    core = index % 2
    chip = index // 2
    quarters = partial.reshape(2, 2, partial.shape[0] // 4, *partial.shape[1:])
    keep = lax.dynamic_index_in_dim(quarters, core, axis=1, keepdims=False)
    send = lax.dynamic_index_in_dim(quarters, 1 - core, axis=1, keepdims=False)
    half = keep + lax.ppermute(send, "af", [(0, 1), (1, 0), (2, 3), (3, 2)])
    keep = lax.dynamic_index_in_dim(half, chip, axis=0, keepdims=False)
    send = lax.dynamic_index_in_dim(half, 1 - chip, axis=0, keepdims=False)
    return keep + lax.ppermute(send, "af", [(0, 2), (2, 0), (1, 3), (3, 1)])


def band_sum(padded, half_width):
    row_count = padded.shape[0] - 2 * half_width
    row_ids = jnp.arange(row_count, dtype=jnp.int32)[:, None]
    col_ids = jnp.arange(padded.shape[0], dtype=jnp.int32)[None, :]
    band_matrix = ((col_ids >= row_ids) & (col_ids <= row_ids + 2 * half_width)).astype(jnp.float32)
    return jnp.dot(
        band_matrix, padded, precision=lax.Precision.HIGHEST, preferred_element_type=jnp.float32
    )


def whiten_local(records, quality):
    local_record = records[0]
    quarter = local_record.shape[0]
    channels = local_record.shape[1]
    parts = lax.axis_size("af")
    band_rows = BINS // parts
    sample_index = lax.axis_index("af") * quarter + jnp.arange(quarter, dtype=jnp.int32)
    basis_table = taper_table(LOWBIN, sample_index, SEGLEN).reshape(2 * BINS, quarter)
    spectra = reduce_scatter_af(
        jnp.dot(basis_table, local_record, preferred_element_type=jnp.float32).reshape(
            BINS, 2, channels
        )
    )
    power_bins = spectra[:, 0] * spectra[:, 0] + spectra[:, 1] * spectra[:, 1]
    padded = extended(power_bins, (("af", 0),), SMOOTH)
    smoothed = band_sum(padded, SMOOTH)
    factor = quality.astype(jnp.float32)[None, :] / jnp.sqrt(
        smoothed * (1.0 / (2 * SMOOTH + 1)) + 1e-06
    )
    return (spectra * factor[:, None, :]).astype(jnp.bfloat16)


def bin_cross(whitened, block):
    segs, _, channels = whitened.shape
    blocks = channels // block
    real_w = whitened[:, 0]
    imag_w = whitened[:, 1]
    right = jnp.concatenate([real_w, imag_w], axis=0)
    left = jnp.stack([right, jnp.concatenate([imag_w, -real_w], axis=0)], axis=0)
    depth = right.shape[0]
    right_pad = jnp.pad(right, ((0, 0), (0, block))).reshape(depth, blocks + 1, block)
    windows = jnp.concatenate([right_pad[:, :blocks], right_pad[:, 1:]], axis=2)
    left_blocks = left.reshape(2, depth, blocks, block)
    gram = jnp.einsum(
        "pkbc,kbe->bcpe", left_blocks, windows, preferred_element_type=jnp.float32
    )
    width = 2 * block
    flat = gram.transpose(0, 2, 1, 3).reshape(blocks, 2, block * width)
    flat = jnp.pad(flat, ((0, 0), (0, 0), (0, block)))
    skew = flat.reshape(blocks, 2, block, width + 1)[:, :, :, : REACH + 1]
    return skew.transpose(0, 2, 3, 1).reshape(channels, REACH + 1, 2)


def per_device(records, quality, band_low, band_high):
    whitened = whiten_local(records, quality)
    band_rows, _, channels = whitened.shape
    slab_count = lax.axis_size("ch")
    slab_width = channels // slab_count
    by_bin = lax.all_to_all(
        whitened.reshape(band_rows, 1, 2, channels),
        "ch",
        split_axis=0,
        concat_axis=1,
        tiled=True,
    )[0]
    segments = by_bin.shape[0]
    cross = bin_cross(by_bin, REACH)
    back = lax.all_to_all(
        cross.astype(jnp.bfloat16).reshape(slab_count, slab_width, REACH + 1, 2),
        "ch",
        split_axis=0,
        concat_axis=0,
        tiled=True,
    ).astype(jnp.float32)
    offsets = jnp.arange(REACH + 1, dtype=jnp.int32)
    inside_band = (
        (offsets[None, :] >= band_low[:, None]) & (offsets[None, :] <= band_high[:, None])
    ).astype(jnp.float32)
    result = (
        jnp.transpose(back, (1, 2, 3, 0))
        * inside_band[:, :, None, None]
        * (1.0 / math.sqrt(segments))
    )
    return result


def solution(mesh):
    return jax.shard_map(
        per_device,
        mesh=mesh,
        in_specs=(P("ch", "af", None), P(), P("ch"), P("ch")),
        out_specs=P("ch", None, None, "af"),
        check_vma=False,
    )
```

```python
import math

import jax
import jax.numpy as jnp
from jax import lax
from jax.sharding import PartitionSpec as P

SEGLEN = 8192
BINS = 512
LOWBIN = 64
SMOOTH = 32
REACH = 128


def extended(cells, sides, width):
    for axis, dim in sides:
        count = lax.axis_size(axis)
        ends = count - 1
        head = lax.slice_in_dim(cells, 0, width, axis=dim)
        tail = lax.slice_in_dim(cells, cells.shape[dim] - width, cells.shape[dim], axis=dim)
        cells = jnp.concatenate(
            [
                lax.ppermute(tail, axis, [(i, (i + 1) % count) for i in range(ends)]),
                cells,
                lax.ppermute(head, axis, [((i + 1) % count, i) for i in range(ends)]),
            ],
            axis=dim,
        )
    return cells


def taper_table(bin_start, sample_index, length):
    fine = 64
    groups = 8
    step = 2.0 * math.pi / length
    coarse_bins = bin_start + fine * jnp.arange(groups, dtype=jnp.int32)
    fine_bins = jnp.arange(fine, dtype=jnp.int32)
    coarse_angle = (coarse_bins[:, None] * sample_index[None, :] % length).astype(jnp.float32) * step
    fine_angle = (fine_bins[:, None] * sample_index[None, :] % length).astype(jnp.float32) * step
    cos_c = jnp.cos(coarse_angle)[:, None, :]
    sin_c = jnp.sin(coarse_angle)[:, None, :]
    cos_f = jnp.cos(fine_angle)[None, :, :]
    sin_f = jnp.sin(fine_angle)[None, :, :]
    rows = groups * fine
    cos_a = (cos_c * cos_f - sin_c * sin_f).reshape(rows, -1)
    sin_a = (sin_c * cos_f + cos_c * sin_f).reshape(rows, -1)
    tapers = 0.5 - 0.5 * jnp.cos(sample_index.astype(jnp.float32) * step)
    real_row = (tapers[None, :] * cos_a).astype(jnp.bfloat16)
    imag_row = (-(tapers[None, :] * sin_a)).astype(jnp.bfloat16)
    return jnp.stack([real_row, imag_row], axis=1)


def reduce_scatter_af(partial):
    index = lax.axis_index("af")
    core = index % 2
    chip = index // 2
    quarters = partial.reshape(2, 2, partial.shape[0] // 4, *partial.shape[1:])
    keep = lax.dynamic_index_in_dim(quarters, core, axis=1, keepdims=False)
    send = lax.dynamic_index_in_dim(quarters, 1 - core, axis=1, keepdims=False)
    half = keep + lax.ppermute(send, "af", [(0, 1), (1, 0), (2, 3), (3, 2)])
    keep = lax.dynamic_index_in_dim(half, chip, axis=0, keepdims=False)
    send = lax.dynamic_index_in_dim(half, 1 - chip, axis=0, keepdims=False)
    return keep + lax.ppermute(send, "af", [(0, 2), (2, 0), (1, 3), (3, 1)])


def band_sum(padded, half_width):
    row_count = padded.shape[0] - 2 * half_width
    row_ids = jnp.arange(row_count, dtype=jnp.int32)[:, None]
    col_ids = jnp.arange(padded.shape[0], dtype=jnp.int32)[None, :]
    band_matrix = ((col_ids >= row_ids) & (col_ids <= row_ids + 2 * half_width)).astype(jnp.float32)
    return jnp.dot(
        band_matrix, padded, precision=lax.Precision.HIGHEST, preferred_element_type=jnp.float32
    )


def whiten_local(records, quality):
    local_record = records[0]
    quarter = local_record.shape[0]
    channels = local_record.shape[1]
    parts = lax.axis_size("af")
    band_rows = BINS // parts
    sample_index = lax.axis_index("af") * quarter + jnp.arange(quarter, dtype=jnp.int32)
    basis_table = taper_table(LOWBIN, sample_index, SEGLEN).reshape(2 * BINS, quarter)
    spectra = reduce_scatter_af(
        jnp.dot(basis_table, local_record, preferred_element_type=jnp.float32).reshape(
            BINS, 2, channels
        )
    )
    power_bins = spectra[:, 0] * spectra[:, 0] + spectra[:, 1] * spectra[:, 1]
    padded = extended(power_bins, (("af", 0),), SMOOTH)
    smoothed = band_sum(padded, SMOOTH)
    factor = quality.astype(jnp.float32)[None, :] / jnp.sqrt(
        smoothed * (1.0 / (2 * SMOOTH + 1)) + 1e-06
    )
    return (spectra * factor[:, None, :]).astype(jnp.bfloat16)


def bin_cross(whitened, block, slab_width):
    segs, _, channels = whitened.shape
    blocks = channels // block
    real_w = whitened[:, 0]
    imag_w = whitened[:, 1]
    right = jnp.concatenate([real_w, imag_w], axis=0)
    left = jnp.stack([right, jnp.concatenate([imag_w, -real_w], axis=0)], axis=0)
    depth = right.shape[0]
    right_pad = jnp.pad(right, ((0, 0), (0, block))).reshape(depth, blocks + 1, block)
    windows = jnp.concatenate([right_pad[:, :blocks], right_pad[:, 1:]], axis=2)
    left_blocks = left.reshape(2, depth, blocks, block)
    gram = jnp.einsum(
        "pkbc,kbe->bpce", left_blocks, windows, preferred_element_type=jnp.float32
    ).astype(jnp.bfloat16)
    width = 2 * block
    flat = gram.reshape(blocks, 2, block * width)
    flat = jnp.pad(flat, ((0, 0), (0, 0), (0, block)))
    skew = flat.reshape(blocks, 2, block, width + 1)[:, :, :, : REACH + 1]
    slabs = block // slab_width
    rows = skew.reshape(blocks, 2, slabs, slab_width * (REACH + 1)).transpose(0, 2, 1, 3)
    return rows.reshape(blocks * slabs, 2 * slab_width * (REACH + 1))


def per_device(records, quality, band_low, band_high):
    whitened = whiten_local(records, quality)
    band_rows, _, channels = whitened.shape
    slab_count = lax.axis_size("ch")
    slab_width = channels // slab_count
    by_bin = lax.all_to_all(
        whitened.reshape(band_rows, 1, 2, channels),
        "ch",
        split_axis=0,
        concat_axis=1,
        tiled=True,
    )[0]
    segments = by_bin.shape[0]
    rows = bin_cross(by_bin, REACH, slab_width)
    back = lax.all_to_all(rows, "ch", split_axis=0, concat_axis=0, tiled=True)
    back = back.reshape(slab_count, 2, slab_width, REACH + 1).astype(jnp.float32)
    offsets = jnp.arange(REACH + 1, dtype=jnp.int32)
    inside_band = (
        (offsets[None, :] >= band_low[:, None]) & (offsets[None, :] <= band_high[:, None])
    ).astype(jnp.float32)
    result = (
        jnp.transpose(back, (2, 3, 1, 0))
        * inside_band[:, :, None, None]
        * (1.0 / math.sqrt(segments))
    )
    return result


def solution(mesh):
    return jax.shard_map(
        per_device,
        mesh=mesh,
        in_specs=(P("ch", "af", None), P(), P("ch"), P("ch")),
        out_specs=P("ch", None, None, "af"),
        check_vma=False,
    )
```

```python
import math

import jax
import jax.numpy as jnp
from jax import lax
from jax.sharding import PartitionSpec as P

SEGLEN = 8192
BINS = 512
LOWBIN = 64
SMOOTH = 32
REACH = 128


def extended(cells, sides, width):
    for axis, dim in sides:
        count = lax.axis_size(axis)
        ends = count - 1
        head = lax.slice_in_dim(cells, 0, width, axis=dim)
        tail = lax.slice_in_dim(cells, cells.shape[dim] - width, cells.shape[dim], axis=dim)
        cells = jnp.concatenate(
            [
                lax.ppermute(tail, axis, [(i, (i + 1) % count) for i in range(ends)]),
                cells,
                lax.ppermute(head, axis, [((i + 1) % count, i) for i in range(ends)]),
            ],
            axis=dim,
        )
    return cells


def taper_table(bin_start, sample_index, length):
    fine = 64
    groups = 8
    step = 2.0 * math.pi / length
    coarse_bins = bin_start + fine * jnp.arange(groups, dtype=jnp.int32)
    fine_bins = jnp.arange(fine, dtype=jnp.int32)
    coarse_angle = (coarse_bins[:, None] * sample_index[None, :] % length).astype(jnp.float32) * step
    fine_angle = (fine_bins[:, None] * sample_index[None, :] % length).astype(jnp.float32) * step
    cos_c = jnp.cos(coarse_angle)[:, None, :]
    sin_c = jnp.sin(coarse_angle)[:, None, :]
    cos_f = jnp.cos(fine_angle)[None, :, :]
    sin_f = jnp.sin(fine_angle)[None, :, :]
    rows = groups * fine
    cos_a = (cos_c * cos_f - sin_c * sin_f).reshape(rows, -1)
    sin_a = (sin_c * cos_f + cos_c * sin_f).reshape(rows, -1)
    tapers = 0.5 - 0.5 * jnp.cos(sample_index.astype(jnp.float32) * step)
    real_row = (tapers[None, :] * cos_a).astype(jnp.bfloat16)
    imag_row = (-(tapers[None, :] * sin_a)).astype(jnp.bfloat16)
    return jnp.stack([real_row, imag_row], axis=1)


def reduce_scatter_af(partial):
    index = lax.axis_index("af")
    core = index % 2
    chip = index // 2
    quarters = partial.reshape(2, 2, partial.shape[0] // 4, *partial.shape[1:])
    keep = lax.dynamic_index_in_dim(quarters, core, axis=1, keepdims=False)
    send = lax.dynamic_index_in_dim(quarters, 1 - core, axis=1, keepdims=False)
    half = keep + lax.ppermute(send, "af", [(0, 1), (1, 0), (2, 3), (3, 2)])
    keep = lax.dynamic_index_in_dim(half, chip, axis=0, keepdims=False)
    send = lax.dynamic_index_in_dim(half, 1 - chip, axis=0, keepdims=False)
    return keep + lax.ppermute(send, "af", [(0, 2), (2, 0), (1, 3), (3, 1)])


def band_sum(padded, half_width):
    row_count = padded.shape[0] - 2 * half_width
    row_ids = jnp.arange(row_count, dtype=jnp.int32)[:, None]
    col_ids = jnp.arange(padded.shape[0], dtype=jnp.int32)[None, :]
    band_matrix = ((col_ids >= row_ids) & (col_ids <= row_ids + 2 * half_width)).astype(jnp.float32)
    return jnp.dot(
        band_matrix, padded, precision=lax.Precision.HIGHEST, preferred_element_type=jnp.float32
    )


def whiten_local(local_record, basis_table, quality):
    channels = local_record.shape[1]
    spectra = reduce_scatter_af(
        jnp.dot(basis_table, local_record, preferred_element_type=jnp.float32).reshape(
            BINS, 2, channels
        )
    )
    power_bins = spectra[:, 0] * spectra[:, 0] + spectra[:, 1] * spectra[:, 1]
    padded = extended(power_bins, (("af", 0),), SMOOTH)
    smoothed = band_sum(padded, SMOOTH)
    factor = quality.astype(jnp.float32)[None, :] / jnp.sqrt(
        smoothed * (1.0 / (2 * SMOOTH + 1)) + 1e-06
    )
    return (spectra * factor[:, None, :]).astype(jnp.bfloat16)


def to_bins(whitened):
    band_rows, _, channels = whitened.shape
    return lax.all_to_all(
        whitened.reshape(band_rows, 1, 2, channels),
        "ch",
        split_axis=0,
        concat_axis=1,
        tiled=True,
    )[0]


def bin_cross(whitened, block, slab_width):
    segs, _, channels = whitened.shape
    blocks = channels // block
    real_w = whitened[:, 0]
    imag_w = whitened[:, 1]
    right = jnp.concatenate([real_w, imag_w], axis=0)
    left = jnp.stack([right, jnp.concatenate([imag_w, -real_w], axis=0)], axis=0)
    depth = right.shape[0]
    right_pad = jnp.pad(right, ((0, 0), (0, block))).reshape(depth, blocks + 1, block)
    windows = jnp.concatenate([right_pad[:, :blocks], right_pad[:, 1:]], axis=2)
    left_blocks = left.reshape(2, depth, blocks, block)
    gram = jnp.einsum(
        "pkbc,kbe->bpce", left_blocks, windows, preferred_element_type=jnp.float32
    ).astype(jnp.bfloat16)
    width = 2 * block
    flat = gram.reshape(blocks, 2, block * width)
    flat = jnp.pad(flat, ((0, 0), (0, 0), (0, block)))
    skew = flat.reshape(blocks, 2, block, width + 1)[:, :, :, : REACH + 1]
    slabs = block // slab_width
    rows = skew.reshape(blocks, 2, slabs, slab_width * (REACH + 1)).transpose(0, 2, 1, 3)
    return rows.reshape(blocks * slabs, 2 * slab_width * (REACH + 1))


def per_device(records, quality, band_low, band_high):
    local_record = records[0]
    quarter, channels = local_record.shape
    sample_index = lax.axis_index("af") * quarter + jnp.arange(quarter, dtype=jnp.int32)
    basis_table = taper_table(LOWBIN, sample_index, SEGLEN).reshape(2 * BINS, quarter)
    chunks = 2
    width = channels // chunks
    pieces = []
    whitened = None
    for chunk in range(chunks):
        part = slice(chunk * width, (chunk + 1) * width)
        chunk_record = local_record[:, part]
        if whitened is not None:
            whitened, chunk_record = lax.optimization_barrier((whitened, chunk_record))
            pieces.append(to_bins(whitened))
        whitened = whiten_local(chunk_record, basis_table, quality[part])
    pieces.append(to_bins(whitened))
    by_bin = jnp.concatenate(pieces, axis=2)
    slab_count = lax.axis_size("ch")
    slab_width = channels // slab_count
    segments = by_bin.shape[0]
    rows = bin_cross(by_bin, REACH, slab_width)
    back = lax.all_to_all(rows, "ch", split_axis=0, concat_axis=0, tiled=True)
    back = back.reshape(slab_count, 2, slab_width, REACH + 1).astype(jnp.float32)
    offsets = jnp.arange(REACH + 1, dtype=jnp.int32)
    inside_band = (
        (offsets[None, :] >= band_low[:, None]) & (offsets[None, :] <= band_high[:, None])
    ).astype(jnp.float32)
    result = (
        jnp.transpose(back, (2, 3, 1, 0))
        * inside_band[:, :, None, None]
        * (1.0 / math.sqrt(segments))
    )
    return result


def solution(mesh):
    return jax.shard_map(
        per_device,
        mesh=mesh,
        in_specs=(P("ch", "af", None), P(), P("ch"), P("ch")),
        out_specs=P("ch", None, None, "af"),
        check_vma=False,
    )
```

```python
import math

import jax
import jax.numpy as jnp
from jax import lax
from jax.sharding import PartitionSpec as P

SEGLEN = 8192
BINS = 512
LOWBIN = 64
SMOOTH = 32
REACH = 128


def extended(cells, sides, width):
    for axis, dim in sides:
        count = lax.axis_size(axis)
        ends = count - 1
        head = lax.slice_in_dim(cells, 0, width, axis=dim)
        tail = lax.slice_in_dim(cells, cells.shape[dim] - width, cells.shape[dim], axis=dim)
        cells = jnp.concatenate(
            [
                lax.ppermute(tail, axis, [(i, (i + 1) % count) for i in range(ends)]),
                cells,
                lax.ppermute(head, axis, [((i + 1) % count, i) for i in range(ends)]),
            ],
            axis=dim,
        )
    return cells


def taper_table(bin_start, sample_index, length):
    fine = 64
    groups = 8
    step = 2.0 * math.pi / length
    coarse_bins = bin_start + fine * jnp.arange(groups, dtype=jnp.int32)
    fine_bins = jnp.arange(fine, dtype=jnp.int32)
    coarse_angle = (coarse_bins[:, None] * sample_index[None, :] % length).astype(jnp.float32) * step
    fine_angle = (fine_bins[:, None] * sample_index[None, :] % length).astype(jnp.float32) * step
    cos_c = jnp.cos(coarse_angle)[:, None, :]
    sin_c = jnp.sin(coarse_angle)[:, None, :]
    cos_f = jnp.cos(fine_angle)[None, :, :]
    sin_f = jnp.sin(fine_angle)[None, :, :]
    rows = groups * fine
    cos_a = (cos_c * cos_f - sin_c * sin_f).reshape(rows, -1)
    sin_a = (sin_c * cos_f + cos_c * sin_f).reshape(rows, -1)
    tapers = 0.5 - 0.5 * jnp.cos(sample_index.astype(jnp.float32) * step)
    real_row = (tapers[None, :] * cos_a).astype(jnp.bfloat16)
    imag_row = (-(tapers[None, :] * sin_a)).astype(jnp.bfloat16)
    return jnp.stack([real_row, imag_row], axis=1)


def reduce_scatter_af(partial):
    index = lax.axis_index("af")
    core = index % 2
    chip = index // 2
    quarters = partial.reshape(2, 2, partial.shape[0] // 4, *partial.shape[1:])
    keep = lax.dynamic_index_in_dim(quarters, core, axis=1, keepdims=False)
    send = lax.dynamic_index_in_dim(quarters, 1 - core, axis=1, keepdims=False)
    half = keep + lax.ppermute(send, "af", [(0, 1), (1, 0), (2, 3), (3, 2)])
    keep = lax.dynamic_index_in_dim(half, chip, axis=0, keepdims=False)
    send = lax.dynamic_index_in_dim(half, 1 - chip, axis=0, keepdims=False)
    return keep + lax.ppermute(send, "af", [(0, 2), (2, 0), (1, 3), (3, 1)])


def band_sum(padded, half_width):
    row_count = padded.shape[0] - 2 * half_width
    row_ids = jnp.arange(row_count, dtype=jnp.int32)[:, None]
    col_ids = jnp.arange(padded.shape[0], dtype=jnp.int32)[None, :]
    band_matrix = ((col_ids >= row_ids) & (col_ids <= row_ids + 2 * half_width)).astype(jnp.float32)
    return jnp.dot(
        band_matrix, padded, precision=lax.Precision.HIGHEST, preferred_element_type=jnp.float32
    )


def whiten_local(records, quality):
    local_record = records[0]
    quarter = local_record.shape[0]
    channels = local_record.shape[1]
    parts = lax.axis_size("af")
    band_rows = BINS // parts
    sample_index = lax.axis_index("af") * quarter + jnp.arange(quarter, dtype=jnp.int32)
    basis_table = taper_table(LOWBIN, sample_index, SEGLEN).reshape(2 * BINS, quarter)
    spectra = reduce_scatter_af(
        jnp.dot(basis_table, local_record, preferred_element_type=jnp.float32).reshape(
            BINS, 2, channels
        )
    )
    power_bins = spectra[:, 0] * spectra[:, 0] + spectra[:, 1] * spectra[:, 1]
    padded = extended(power_bins, (("af", 0),), SMOOTH)
    smoothed = band_sum(padded, SMOOTH)
    factor = quality.astype(jnp.float32)[None, :] / jnp.sqrt(
        smoothed * (1.0 / (2 * SMOOTH + 1)) + 1e-06
    )
    return (spectra * factor[:, None, :]).astype(jnp.bfloat16)


def bin_cross(whitened, block, slab_width):
    segs, _, channels = whitened.shape
    blocks = channels // block
    real_w = whitened[:, 0]
    imag_w = whitened[:, 1]
    right = jnp.concatenate([real_w, imag_w], axis=0)
    left = jnp.stack([right, jnp.concatenate([imag_w, -real_w], axis=0)], axis=0)
    depth = right.shape[0]
    right_pad = jnp.pad(right, ((0, 0), (0, block))).reshape(depth, blocks + 1, block)
    windows = jnp.concatenate([right_pad[:, :blocks], right_pad[:, 1:]], axis=2)
    left_blocks = left.reshape(2, depth, blocks, block)
    gram = jnp.einsum(
        "pkbc,kbe->bpce", left_blocks, windows, preferred_element_type=jnp.float32
    ).astype(jnp.bfloat16)
    width = 2 * block
    flat = gram.reshape(blocks, 2, block * width)
    flat = jnp.pad(flat, ((0, 0), (0, 0), (0, block)))
    skew = flat.reshape(blocks, 2, block, width + 1)[:, :, :, : REACH + 1]
    slabs = block // slab_width
    rows = skew.reshape(blocks, 2, slabs, slab_width * (REACH + 1)).transpose(0, 2, 1, 3)
    return rows.reshape(blocks * slabs, 2, slab_width * (REACH + 1))


def per_device(records, quality, band_low, band_high):
    whitened = whiten_local(records, quality)
    band_rows, _, channels = whitened.shape
    slab_count = lax.axis_size("ch")
    slab_width = channels // slab_count
    by_bin = lax.all_to_all(
        whitened.reshape(band_rows, 1, 2, channels),
        "ch",
        split_axis=0,
        concat_axis=1,
        tiled=True,
    )[0]
    segments = by_bin.shape[0]
    rows = bin_cross(by_bin, REACH, slab_width)
    back = lax.all_to_all(rows, "ch", split_axis=0, concat_axis=0, tiled=True)
    back = back.reshape(slab_count, 2, slab_width, REACH + 1).astype(jnp.float32)
    offsets = jnp.arange(REACH + 1, dtype=jnp.int32)
    inside_band = (
        (offsets[None, :] >= band_low[:, None]) & (offsets[None, :] <= band_high[:, None])
    ).astype(jnp.float32)
    result = (
        jnp.transpose(back, (2, 3, 1, 0))
        * inside_band[:, :, None, None]
        * (1.0 / math.sqrt(segments))
    )
    return result


def solution(mesh):
    return jax.shard_map(
        per_device,
        mesh=mesh,
        in_specs=(P("ch", "af", None), P(), P("ch"), P("ch")),
        out_specs=P("ch", None, None, "af"),
        check_vma=False,
    )
```

```python
import math

import jax
import jax.numpy as jnp
from jax import lax
from jax.sharding import PartitionSpec as P

SEGLEN = 8192
BINS = 512
LOWBIN = 64
SMOOTH = 32
REACH = 128


def extended(cells, sides, width):
    for axis, dim in sides:
        count = lax.axis_size(axis)
        ends = count - 1
        head = lax.slice_in_dim(cells, 0, width, axis=dim)
        tail = lax.slice_in_dim(cells, cells.shape[dim] - width, cells.shape[dim], axis=dim)
        cells = jnp.concatenate(
            [
                lax.ppermute(tail, axis, [(i, (i + 1) % count) for i in range(ends)]),
                cells,
                lax.ppermute(head, axis, [((i + 1) % count, i) for i in range(ends)]),
            ],
            axis=dim,
        )
    return cells


def fine_rotation(sample_index, length, fine):
    step = 2.0 * math.pi / length
    fine_bins = jnp.arange(fine, dtype=jnp.int32)
    fine_angle = (fine_bins[:, None] * sample_index[None, :] % length).astype(jnp.float32) * step
    tapers = 0.5 - 0.5 * jnp.cos(sample_index.astype(jnp.float32) * step)
    return jnp.cos(fine_angle)[None], jnp.sin(fine_angle)[None], tapers


def taper_table(coarse_bins, sample_index, length, fine_table):
    cos_f, sin_f, tapers = fine_table
    step = 2.0 * math.pi / length
    coarse_angle = (coarse_bins[:, None] * sample_index[None, :] % length).astype(jnp.float32) * step
    cos_c = jnp.cos(coarse_angle)[:, None, :]
    sin_c = jnp.sin(coarse_angle)[:, None, :]
    rows = coarse_bins.shape[0] * cos_f.shape[1]
    cos_a = (cos_c * cos_f - sin_c * sin_f).reshape(rows, -1)
    sin_a = (sin_c * cos_f + cos_c * sin_f).reshape(rows, -1)
    real_row = (tapers[None, :] * cos_a).astype(jnp.bfloat16)
    imag_row = (-(tapers[None, :] * sin_a)).astype(jnp.bfloat16)
    return jnp.stack([real_row, imag_row], axis=1)


def quarter_spectra(local_record, sample_index, quarter_index, fine_table):
    fine = fine_table[0].shape[1]
    rows = BINS // 4
    coarse_bins = LOWBIN + quarter_index * rows + fine * jnp.arange(rows // fine, dtype=jnp.int32)
    basis = taper_table(coarse_bins, sample_index, SEGLEN, fine_table).reshape(2 * rows, -1)
    out = jnp.dot(basis, local_record, preferred_element_type=jnp.float32)
    return out.reshape(rows, 2, local_record.shape[1])


def reduced_spectra(local_record):
    quarter = local_record.shape[0]
    index = lax.axis_index("af")
    core = index % 2
    chip = index // 2
    sample_index = index * quarter + jnp.arange(quarter, dtype=jnp.int32)
    fine_table = fine_rotation(sample_index, SEGLEN, 64)
    cores = [(0, 1), (1, 0), (2, 3), (3, 2)]
    chips = [(0, 2), (2, 0), (1, 3), (3, 1)]

    def spectra_of(q_chip, q_core):
        return quarter_spectra(local_record, sample_index, 2 * q_chip + q_core, fine_table)

    first = lax.ppermute(spectra_of(1 - chip, 1 - core), "af", cores)
    second = lax.ppermute(spectra_of(chip, 1 - core), "af", cores)
    outgoing = spectra_of(1 - chip, core) + first
    incoming = lax.ppermute(outgoing, "af", chips)
    return (spectra_of(chip, core) + second) + incoming


def band_sum(padded, half_width):
    row_count = padded.shape[0] - 2 * half_width
    row_ids = jnp.arange(row_count, dtype=jnp.int32)[:, None]
    col_ids = jnp.arange(padded.shape[0], dtype=jnp.int32)[None, :]
    band_matrix = ((col_ids >= row_ids) & (col_ids <= row_ids + 2 * half_width)).astype(jnp.float32)
    return jnp.dot(
        band_matrix, padded, precision=lax.Precision.HIGHEST, preferred_element_type=jnp.float32
    )


def whiten_local(records, quality):
    spectra = reduced_spectra(records[0])
    power_bins = spectra[:, 0] * spectra[:, 0] + spectra[:, 1] * spectra[:, 1]
    padded = extended(power_bins, (("af", 0),), SMOOTH)
    smoothed = band_sum(padded, SMOOTH)
    factor = quality.astype(jnp.float32)[None, :] / jnp.sqrt(
        smoothed * (1.0 / (2 * SMOOTH + 1)) + 1e-06
    )
    return (spectra * factor[:, None, :]).astype(jnp.bfloat16)


def bin_cross(whitened, block, slab_width):
    segs, _, channels = whitened.shape
    blocks = channels // block
    real_w = whitened[:, 0]
    imag_w = whitened[:, 1]
    right = jnp.concatenate([real_w, imag_w], axis=0)
    left = jnp.stack([right, jnp.concatenate([imag_w, -real_w], axis=0)], axis=0)
    depth = right.shape[0]
    right_pad = jnp.pad(right, ((0, 0), (0, block))).reshape(depth, blocks + 1, block)
    windows = jnp.concatenate([right_pad[:, :blocks], right_pad[:, 1:]], axis=2)
    left_blocks = left.reshape(2, depth, blocks, block)
    gram = jnp.einsum(
        "pkbc,kbe->bpce", left_blocks, windows, preferred_element_type=jnp.float32
    ).astype(jnp.bfloat16)
    width = 2 * block
    flat = gram.reshape(blocks, 2, block * width)
    flat = jnp.pad(flat, ((0, 0), (0, 0), (0, block)))
    skew = flat.reshape(blocks, 2, block, width + 1)[:, :, :, : REACH + 1]
    slabs = block // slab_width
    rows = skew.reshape(blocks, 2, slabs, slab_width * (REACH + 1)).transpose(0, 2, 1, 3)
    return rows.reshape(blocks * slabs, 2, slab_width * (REACH + 1))


def per_device(records, quality, band_low, band_high):
    whitened = whiten_local(records, quality)
    band_rows, _, channels = whitened.shape
    slab_count = lax.axis_size("ch")
    slab_width = channels // slab_count
    by_bin = lax.all_to_all(
        whitened.reshape(band_rows, 1, 2, channels),
        "ch",
        split_axis=0,
        concat_axis=1,
        tiled=True,
    )[0]
    segments = by_bin.shape[0]
    rows = bin_cross(by_bin, REACH, slab_width)
    back = lax.all_to_all(rows, "ch", split_axis=0, concat_axis=0, tiled=True)
    back = back.reshape(slab_count, 2, slab_width, REACH + 1).astype(jnp.float32)
    offsets = jnp.arange(REACH + 1, dtype=jnp.int32)
    inside_band = (
        (offsets[None, :] >= band_low[:, None]) & (offsets[None, :] <= band_high[:, None])
    ).astype(jnp.float32)
    result = (
        jnp.transpose(back, (2, 3, 1, 0))
        * inside_band[:, :, None, None]
        * (1.0 / math.sqrt(segments))
    )
    return result


def solution(mesh):
    return jax.shard_map(
        per_device,
        mesh=mesh,
        in_specs=(P("ch", "af", None), P(), P("ch"), P("ch")),
        out_specs=P("ch", None, None, "af"),
        check_vma=False,
    )
```

```python
import math

import jax
import jax.numpy as jnp
from jax import lax
from jax.sharding import PartitionSpec as P

SEGLEN = 8192
BINS = 512
LOWBIN = 64
SMOOTH = 32
REACH = 128


def extended(cells, sides, width):
    for axis, dim in sides:
        count = lax.axis_size(axis)
        ends = count - 1
        head = lax.slice_in_dim(cells, 0, width, axis=dim)
        tail = lax.slice_in_dim(cells, cells.shape[dim] - width, cells.shape[dim], axis=dim)
        cells = jnp.concatenate(
            [
                lax.ppermute(tail, axis, [(i, (i + 1) % count) for i in range(ends)]),
                cells,
                lax.ppermute(head, axis, [((i + 1) % count, i) for i in range(ends)]),
            ],
            axis=dim,
        )
    return cells


def fine_rotation(sample_index, length, fine):
    step = 2.0 * math.pi / length
    fine_bins = jnp.arange(fine, dtype=jnp.int32)
    fine_angle = (fine_bins[:, None] * sample_index[None, :] % length).astype(jnp.float32) * step
    tapers = 0.5 - 0.5 * jnp.cos(sample_index.astype(jnp.float32) * step)
    return jnp.cos(fine_angle)[None], jnp.sin(fine_angle)[None], tapers


def taper_table(coarse_bins, sample_index, length, fine_table):
    cos_f, sin_f, tapers = fine_table
    step = 2.0 * math.pi / length
    coarse_angle = (coarse_bins[:, None] * sample_index[None, :] % length).astype(jnp.float32) * step
    cos_c = jnp.cos(coarse_angle)[:, None, :]
    sin_c = jnp.sin(coarse_angle)[:, None, :]
    rows = coarse_bins.shape[0] * cos_f.shape[1]
    cos_a = (cos_c * cos_f - sin_c * sin_f).reshape(rows, -1)
    sin_a = (sin_c * cos_f + cos_c * sin_f).reshape(rows, -1)
    real_row = (tapers[None, :] * cos_a).astype(jnp.bfloat16)
    imag_row = (-(tapers[None, :] * sin_a)).astype(jnp.bfloat16)
    return jnp.stack([real_row, imag_row], axis=1)


def quarter_spectra(local_record, sample_index, quarter_index, fine_table):
    fine = fine_table[0].shape[1]
    rows = BINS // 4
    coarse_bins = LOWBIN + quarter_index * rows + fine * jnp.arange(rows // fine, dtype=jnp.int32)
    basis = taper_table(coarse_bins, sample_index, SEGLEN, fine_table).reshape(2 * rows, -1)
    out = jnp.dot(basis, local_record, preferred_element_type=jnp.float32)
    return out.reshape(rows, 2, local_record.shape[1])


def reduced_spectra(local_record):
    quarter = local_record.shape[0]
    index = lax.axis_index("af")
    core = index % 2
    chip = index // 2
    sample_index = index * quarter + jnp.arange(quarter, dtype=jnp.int32)
    fine_table = fine_rotation(sample_index, SEGLEN, 32)
    cores = [(0, 1), (1, 0), (2, 3), (3, 2)]
    chips = [(0, 2), (2, 0), (1, 3), (3, 1)]

    def spectra_of(q_chip, q_core):
        return quarter_spectra(local_record, sample_index, 2 * q_chip + q_core, fine_table)

    first = lax.ppermute(spectra_of(1 - chip, 1 - core), "af", cores)
    second = lax.ppermute(spectra_of(chip, 1 - core), "af", cores)
    outgoing = spectra_of(1 - chip, core) + first
    incoming = lax.ppermute(outgoing, "af", chips)
    return (spectra_of(chip, core) + second) + incoming


def band_sum(padded, half_width):
    row_count = padded.shape[0] - 2 * half_width
    row_ids = jnp.arange(row_count, dtype=jnp.int32)[:, None]
    col_ids = jnp.arange(padded.shape[0], dtype=jnp.int32)[None, :]
    band_matrix = ((col_ids >= row_ids) & (col_ids <= row_ids + 2 * half_width)).astype(jnp.float32)
    return jnp.dot(
        band_matrix, padded, precision=lax.Precision.HIGHEST, preferred_element_type=jnp.float32
    )


def whiten_local(records, quality):
    spectra = reduced_spectra(records[0])
    power_bins = spectra[:, 0] * spectra[:, 0] + spectra[:, 1] * spectra[:, 1]
    padded = extended(power_bins, (("af", 0),), SMOOTH)
    smoothed = band_sum(padded, SMOOTH)
    factor = quality.astype(jnp.float32)[None, :] / jnp.sqrt(
        smoothed * (1.0 / (2 * SMOOTH + 1)) + 1e-06
    )
    return (spectra * factor[:, None, :]).astype(jnp.bfloat16)


def bin_cross(whitened, block, slab_width):
    segs, _, channels = whitened.shape
    blocks = channels // block
    real_w = whitened[:, 0]
    imag_w = whitened[:, 1]
    right = jnp.concatenate([real_w, imag_w], axis=0)
    left = jnp.stack([right, jnp.concatenate([imag_w, -real_w], axis=0)], axis=0)
    depth = right.shape[0]
    right_pad = jnp.pad(right, ((0, 0), (0, block))).reshape(depth, blocks + 1, block)
    windows = jnp.concatenate([right_pad[:, :blocks], right_pad[:, 1:]], axis=2)
    left_blocks = left.reshape(2, depth, blocks, block)
    gram = jnp.einsum(
        "pkbc,kbe->bpce", left_blocks, windows, preferred_element_type=jnp.float32
    ).astype(jnp.bfloat16)
    width = 2 * block
    flat = gram.reshape(blocks, 2, block * width)
    flat = jnp.pad(flat, ((0, 0), (0, 0), (0, block)))
    skew = flat.reshape(blocks, 2, block, width + 1)[:, :, :, : REACH + 1]
    slabs = block // slab_width
    rows = skew.reshape(blocks, 2, slabs, slab_width * (REACH + 1)).transpose(0, 2, 1, 3)
    return rows.reshape(blocks * slabs, 2, slab_width * (REACH + 1))


def per_device(records, quality, band_low, band_high):
    whitened = whiten_local(records, quality)
    band_rows, _, channels = whitened.shape
    slab_count = lax.axis_size("ch")
    slab_width = channels // slab_count
    by_bin = lax.all_to_all(
        whitened.reshape(band_rows, 1, 2, channels),
        "ch",
        split_axis=0,
        concat_axis=1,
        tiled=True,
    )[0]
    segments = by_bin.shape[0]
    rows = bin_cross(by_bin, REACH, slab_width)
    back = lax.all_to_all(rows, "ch", split_axis=0, concat_axis=0, tiled=True)
    back = back.reshape(slab_count, 2, slab_width, REACH + 1)
    back = jnp.transpose(back, (2, 3, 1, 0)).astype(jnp.float32)
    offsets = jnp.arange(REACH + 1, dtype=jnp.int32)
    inside_band = (
        (offsets[None, :] >= band_low[:, None]) & (offsets[None, :] <= band_high[:, None])
    ).astype(jnp.float32)
    result = (
        back
        * inside_band[:, :, None, None]
        * (1.0 / math.sqrt(segments))
    )
    return result


def solution(mesh):
    return jax.shard_map(
        per_device,
        mesh=mesh,
        in_specs=(P("ch", "af", None), P(), P("ch"), P("ch")),
        out_specs=P("ch", None, None, "af"),
        check_vma=False,
    )
```

```python
import math

import jax
import jax.numpy as jnp
from jax import lax
from jax.sharding import PartitionSpec as P

SEGLEN = 8192
BINS = 512
LOWBIN = 64
SMOOTH = 32
REACH = 128


def extended(cells, sides, width):
    for axis, dim in sides:
        count = lax.axis_size(axis)
        ends = count - 1
        head = lax.slice_in_dim(cells, 0, width, axis=dim)
        tail = lax.slice_in_dim(cells, cells.shape[dim] - width, cells.shape[dim], axis=dim)
        cells = jnp.concatenate(
            [
                lax.ppermute(tail, axis, [(i, (i + 1) % count) for i in range(ends)]),
                cells,
                lax.ppermute(head, axis, [((i + 1) % count, i) for i in range(ends)]),
            ],
            axis=dim,
        )
    return cells


def fine_rotation(sample_index, length, fine):
    step = 2.0 * math.pi / length
    fine_bins = jnp.arange(fine, dtype=jnp.int32)
    fine_angle = (fine_bins[:, None] * sample_index[None, :] % length).astype(jnp.float32) * step
    tapers = 0.5 - 0.5 * jnp.cos(sample_index.astype(jnp.float32) * step)
    return jnp.cos(fine_angle)[None], jnp.sin(fine_angle)[None], tapers


def taper_table(coarse_bins, sample_index, length, fine_table):
    cos_f, sin_f, tapers = fine_table
    step = 2.0 * math.pi / length
    coarse_angle = (coarse_bins[:, None] * sample_index[None, :] % length).astype(jnp.float32) * step
    cos_c = jnp.cos(coarse_angle)[:, None, :]
    sin_c = jnp.sin(coarse_angle)[:, None, :]
    rows = coarse_bins.shape[0] * cos_f.shape[1]
    cos_a = (cos_c * cos_f - sin_c * sin_f).reshape(rows, -1)
    sin_a = (sin_c * cos_f + cos_c * sin_f).reshape(rows, -1)
    real_row = (tapers[None, :] * cos_a).astype(jnp.bfloat16)
    imag_row = (-(tapers[None, :] * sin_a)).astype(jnp.bfloat16)
    return jnp.stack([real_row, imag_row], axis=1)


def quarter_spectra(local_record, sample_index, quarter_index, fine_table):
    fine = fine_table[0].shape[1]
    rows = BINS // 4
    coarse_bins = LOWBIN + quarter_index * rows + fine * jnp.arange(rows // fine, dtype=jnp.int32)
    basis = taper_table(coarse_bins, sample_index, SEGLEN, fine_table).reshape(2 * rows, -1)
    out = jnp.dot(basis, local_record, preferred_element_type=jnp.float32)
    return out.reshape(rows, 2, local_record.shape[1])


def reduced_spectra(local_record):
    quarter = local_record.shape[0]
    index = lax.axis_index("af")
    core = index % 2
    chip = index // 2
    sample_index = index * quarter + jnp.arange(quarter, dtype=jnp.int32)
    fine_table = fine_rotation(sample_index, SEGLEN, 32)
    cores = [(0, 1), (1, 0), (2, 3), (3, 2)]
    chips = [(0, 2), (2, 0), (1, 3), (3, 1)]

    def spectra_of(q_chip, q_core):
        return quarter_spectra(local_record, sample_index, 2 * q_chip + q_core, fine_table)

    first = lax.ppermute(spectra_of(1 - chip, 1 - core), "af", cores)
    second = lax.ppermute(spectra_of(chip, 1 - core), "af", cores)
    outgoing = spectra_of(1 - chip, core) + first
    rows = outgoing.shape[0]
    edge_rows = jnp.concatenate([outgoing[:SMOOTH], outgoing[rows - SMOOTH:]], axis=0)
    incoming_edges = lax.ppermute(edge_rows, "af", chips)
    incoming_middle = lax.ppermute(outgoing[SMOOTH : rows - SMOOTH], "af", chips)
    own = spectra_of(chip, core) + second
    own_edges = jnp.concatenate([own[:SMOOTH], own[rows - SMOOTH:]], axis=0)
    edges = own_edges + incoming_edges
    middle = own[SMOOTH : rows - SMOOTH] + incoming_middle
    return edges, middle


def band_sum(padded, half_width):
    row_count = padded.shape[0] - 2 * half_width
    row_ids = jnp.arange(row_count, dtype=jnp.int32)[:, None]
    col_ids = jnp.arange(padded.shape[0], dtype=jnp.int32)[None, :]
    band_matrix = ((col_ids >= row_ids) & (col_ids <= row_ids + 2 * half_width)).astype(jnp.float32)
    return jnp.dot(
        band_matrix, padded, precision=lax.Precision.HIGHEST, preferred_element_type=jnp.float32
    )


def whiten_local(records, quality):
    edges, middle = reduced_spectra(records[0])
    spectra = jnp.concatenate([edges[:SMOOTH], middle, edges[SMOOTH:]], axis=0)
    edge_power = edges[:, 0] * edges[:, 0] + edges[:, 1] * edges[:, 1]
    middle_power = middle[:, 0] * middle[:, 0] + middle[:, 1] * middle[:, 1]
    count = lax.axis_size("af")
    below = lax.ppermute(edge_power[SMOOTH:], "af", [(i, i + 1) for i in range(count - 1)])
    above = lax.ppermute(edge_power[:SMOOTH], "af", [(i + 1, i) for i in range(count - 1)])
    padded = jnp.concatenate(
        [below, edge_power[:SMOOTH], middle_power, edge_power[SMOOTH:], above], axis=0
    )
    smoothed = band_sum(padded, SMOOTH)
    factor = quality.astype(jnp.float32)[None, :] / jnp.sqrt(
        smoothed * (1.0 / (2 * SMOOTH + 1)) + 1e-06
    )
    return (spectra * factor[:, None, :]).astype(jnp.bfloat16)


def bin_cross(whitened, block, slab_width):
    segs, _, channels = whitened.shape
    blocks = channels // block
    real_w = whitened[:, 0]
    imag_w = whitened[:, 1]
    right = jnp.concatenate([real_w, imag_w], axis=0)
    left = jnp.stack([right, jnp.concatenate([imag_w, -real_w], axis=0)], axis=0)
    depth = right.shape[0]
    right_pad = jnp.pad(right, ((0, 0), (0, block))).reshape(depth, blocks + 1, block)
    windows = jnp.concatenate([right_pad[:, :blocks], right_pad[:, 1:]], axis=2)
    left_blocks = left.reshape(2, depth, blocks, block)
    gram = jnp.einsum(
        "pkbc,kbe->bpce", left_blocks, windows, preferred_element_type=jnp.float32
    ).astype(jnp.bfloat16)
    width = 2 * block
    flat = gram.reshape(blocks, 2, block * width)
    flat = jnp.pad(flat, ((0, 0), (0, 0), (0, block)))
    skew = flat.reshape(blocks, 2, block, width + 1)[:, :, :, : REACH + 1]
    slabs = block // slab_width
    rows = skew.reshape(blocks, 2, slabs, slab_width * (REACH + 1)).transpose(0, 2, 1, 3)
    return rows.reshape(blocks * slabs, 2, slab_width * (REACH + 1))


def per_device(records, quality, band_low, band_high):
    whitened = whiten_local(records, quality)
    band_rows, _, channels = whitened.shape
    slab_count = lax.axis_size("ch")
    slab_width = channels // slab_count
    by_bin = lax.all_to_all(
        whitened.reshape(band_rows, 1, 2, channels),
        "ch",
        split_axis=0,
        concat_axis=1,
        tiled=True,
    )[0]
    segments = by_bin.shape[0]
    rows = bin_cross(by_bin, REACH, slab_width)
    back = lax.all_to_all(rows, "ch", split_axis=0, concat_axis=0, tiled=True)
    back = back.reshape(slab_count, 2, slab_width, REACH + 1)
    back = jnp.transpose(back, (2, 3, 1, 0)).astype(jnp.float32)
    offsets = jnp.arange(REACH + 1, dtype=jnp.int32)
    inside_band = (
        (offsets[None, :] >= band_low[:, None]) & (offsets[None, :] <= band_high[:, None])
    ).astype(jnp.float32)
    result = (
        back
        * inside_band[:, :, None, None]
        * (1.0 / math.sqrt(segments))
    )
    return result


def solution(mesh):
    return jax.shard_map(
        per_device,
        mesh=mesh,
        in_specs=(P("ch", "af", None), P(), P("ch"), P("ch")),
        out_specs=P("ch", None, None, "af"),
        check_vma=False,
    )
```

```python
import math

import jax
import jax.numpy as jnp
from jax import lax
from jax.sharding import PartitionSpec as P

SEGLEN = 8192
BINS = 512
LOWBIN = 64
SMOOTH = 32
REACH = 128


def extended(cells, sides, width):
    for axis, dim in sides:
        count = lax.axis_size(axis)
        ends = count - 1
        head = lax.slice_in_dim(cells, 0, width, axis=dim)
        tail = lax.slice_in_dim(cells, cells.shape[dim] - width, cells.shape[dim], axis=dim)
        cells = jnp.concatenate(
            [
                lax.ppermute(tail, axis, [(i, (i + 1) % count) for i in range(ends)]),
                cells,
                lax.ppermute(head, axis, [((i + 1) % count, i) for i in range(ends)]),
            ],
            axis=dim,
        )
    return cells


def rotation_tables(sample_index, length, fine, groups):
    step = 2.0 * math.pi / length
    bins = jnp.concatenate(
        [jnp.arange(fine, dtype=jnp.int32), LOWBIN + fine * jnp.arange(groups, dtype=jnp.int32)]
    )
    angle = (bins[:, None] * sample_index[None, :] % length).astype(jnp.float32) * step
    tapers = 0.5 - 0.5 * jnp.cos(sample_index.astype(jnp.float32) * step)
    return jnp.cos(angle), jnp.sin(angle), tapers


def quarter_spectra(local_record, quarter_index, tables, fine):
    cos_all, sin_all, tapers = tables
    rows = BINS // 4
    per_quarter = rows // fine
    start = fine + quarter_index * per_quarter
    cos_c = lax.dynamic_slice_in_dim(cos_all, start, per_quarter, axis=0)[:, None, :]
    sin_c = lax.dynamic_slice_in_dim(sin_all, start, per_quarter, axis=0)[:, None, :]
    cos_f = cos_all[None, :fine]
    sin_f = sin_all[None, :fine]
    cos_a = (cos_c * cos_f - sin_c * sin_f).reshape(rows, -1)
    sin_a = (sin_c * cos_f + cos_c * sin_f).reshape(rows, -1)
    real_row = (tapers[None, :] * cos_a).astype(jnp.bfloat16)
    imag_row = (-(tapers[None, :] * sin_a)).astype(jnp.bfloat16)
    basis = jnp.stack([real_row, imag_row], axis=1).reshape(2 * rows, -1)
    out = jnp.dot(basis, local_record, preferred_element_type=jnp.float32)
    return out.reshape(rows, 2, local_record.shape[1])


def reduced_spectra(local_record):
    quarter = local_record.shape[0]
    index = lax.axis_index("af")
    core = index % 2
    chip = index // 2
    sample_index = index * quarter + jnp.arange(quarter, dtype=jnp.int32)
    fine = 32
    tables = rotation_tables(sample_index, SEGLEN, fine, BINS // fine)
    cores = [(0, 1), (1, 0), (2, 3), (3, 2)]
    chips = [(0, 2), (2, 0), (1, 3), (3, 1)]

    def spectra_of(q_chip, q_core):
        return quarter_spectra(local_record, 2 * q_chip + q_core, tables, fine)

    first = lax.ppermute(spectra_of(1 - chip, 1 - core), "af", cores)
    second = lax.ppermute(spectra_of(chip, 1 - core), "af", cores)
    outgoing = spectra_of(1 - chip, core) + first
    rows = outgoing.shape[0]
    edge_rows = jnp.concatenate([outgoing[:SMOOTH], outgoing[rows - SMOOTH:]], axis=0)
    incoming_edges = lax.ppermute(edge_rows, "af", chips)
    incoming_middle = lax.ppermute(outgoing[SMOOTH : rows - SMOOTH], "af", chips)
    own = spectra_of(chip, core) + second
    own_edges = jnp.concatenate([own[:SMOOTH], own[rows - SMOOTH:]], axis=0)
    edges = own_edges + incoming_edges
    middle = own[SMOOTH : rows - SMOOTH] + incoming_middle
    return edges, middle


def band_sum(padded, half_width):
    row_count = padded.shape[0] - 2 * half_width
    row_ids = jnp.arange(row_count, dtype=jnp.int32)[:, None]
    col_ids = jnp.arange(padded.shape[0], dtype=jnp.int32)[None, :]
    band_matrix = ((col_ids >= row_ids) & (col_ids <= row_ids + 2 * half_width)).astype(jnp.float32)
    return jnp.dot(
        band_matrix, padded, precision=lax.Precision.HIGHEST, preferred_element_type=jnp.float32
    )


def whiten_local(records, quality):
    edges, middle = reduced_spectra(records[0])
    spectra = jnp.concatenate([edges[:SMOOTH], middle, edges[SMOOTH:]], axis=0)
    edge_power = edges[:, 0] * edges[:, 0] + edges[:, 1] * edges[:, 1]
    middle_power = middle[:, 0] * middle[:, 0] + middle[:, 1] * middle[:, 1]
    count = lax.axis_size("af")
    below = lax.ppermute(edge_power[SMOOTH:], "af", [(i, i + 1) for i in range(count - 1)])
    above = lax.ppermute(edge_power[:SMOOTH], "af", [(i + 1, i) for i in range(count - 1)])
    padded = jnp.concatenate(
        [below, edge_power[:SMOOTH], middle_power, edge_power[SMOOTH:], above], axis=0
    )
    smoothed = band_sum(padded, SMOOTH)
    factor = quality.astype(jnp.float32)[None, :] / jnp.sqrt(
        smoothed * (1.0 / (2 * SMOOTH + 1)) + 1e-06
    )
    return (spectra * factor[:, None, :]).astype(jnp.bfloat16)


def bin_cross(whitened, block, slab_width):
    segs, _, channels = whitened.shape
    blocks = channels // block
    real_w = whitened[:, 0]
    imag_w = whitened[:, 1]
    right = jnp.concatenate([real_w, imag_w], axis=0)
    left = jnp.stack([right, jnp.concatenate([imag_w, -real_w], axis=0)], axis=0)
    depth = right.shape[0]
    right_pad = jnp.pad(right, ((0, 0), (0, block))).reshape(depth, blocks + 1, block)
    windows = jnp.concatenate([right_pad[:, :blocks], right_pad[:, 1:]], axis=2)
    left_blocks = left.reshape(2, depth, blocks, block)
    gram = jnp.einsum(
        "pkbc,kbe->bpce", left_blocks, windows, preferred_element_type=jnp.float32
    ).astype(jnp.bfloat16)
    width = 2 * block
    flat = gram.reshape(blocks, 2, block * width)
    flat = jnp.pad(flat, ((0, 0), (0, 0), (0, block)))
    skew = flat.reshape(blocks, 2, block, width + 1)[:, :, :, : REACH + 1]
    slabs = block // slab_width
    rows = skew.reshape(blocks, 2, slabs, slab_width * (REACH + 1)).transpose(0, 2, 1, 3)
    return rows.reshape(blocks * slabs, 2, slab_width * (REACH + 1))


def per_device(records, quality, band_low, band_high):
    whitened = whiten_local(records, quality)
    band_rows, _, channels = whitened.shape
    slab_count = lax.axis_size("ch")
    slab_width = channels // slab_count
    by_bin = lax.all_to_all(
        whitened.reshape(band_rows, 1, 2, channels),
        "ch",
        split_axis=0,
        concat_axis=1,
        tiled=True,
    )[0]
    segments = by_bin.shape[0]
    rows = bin_cross(by_bin, REACH, slab_width)
    back = lax.all_to_all(rows, "ch", split_axis=0, concat_axis=0, tiled=True)
    back = back.reshape(slab_count, 2, slab_width, REACH + 1)
    back = jnp.transpose(back, (2, 3, 1, 0)).astype(jnp.float32)
    offsets = jnp.arange(REACH + 1, dtype=jnp.int32)
    inside_band = (
        (offsets[None, :] >= band_low[:, None]) & (offsets[None, :] <= band_high[:, None])
    ).astype(jnp.float32)
    result = (
        back
        * inside_band[:, :, None, None]
        * (1.0 / math.sqrt(segments))
    )
    return result


def solution(mesh):
    return jax.shard_map(
        per_device,
        mesh=mesh,
        in_specs=(P("ch", "af", None), P(), P("ch"), P("ch")),
        out_specs=P("ch", None, None, "af"),
        check_vma=False,
    )
```
